512 devices in a mesh: axial: 64 (over y_hi, z, core), circ: 8 (over x, y_lo).
Axes of the slice: x: 4, y: 8 (y_hi: 4, y_lo: 2; y = y_hi * 2 + y_lo), z: 8, core: 2. Of those that a mesh axis runs over, the one named last changes fastest.
Arguments:
- mode_shapes: float32 [128, 16, 128, 512], P('axial', 'circ'), may hold values from -0.03125 to 0.03125
- amplitude: float32 [128, 16, 128], P('axial', 'circ'), may hold values from 0.3 to 3
- pair_list: int32 [64, 8, 3, 20], P('axial', 'circ'), may hold values from -1 to 3, as said below
- pair_counts: int32 [64, 8], P('axial', 'circ'), may hold values from 2 to 20, as said below
Outputs:
- modal_spectrum: float32 [2, 512, 512], P(None, 'axial', 'circ')
The draws below stay inside these ranges and needn't reach their ends.
Inputs may be any that keep to these rules, and one draw needn't show every extreme that they name: `pair_list`: each device's 20 slots hold distinct pairs, and each of its local blocks is the row block of exactly five slots, one for each of the five offsets. Entry 0 is the row block's local index i * 2 + j of the device's 2 x 2 blocks, entry 1 the axial offset (0 or 1), entry 2 the circumferential offset (-1, 0 or 1), and an axial offset 0 comes only with a circumferential offset of 0 or 1. `pair_counts`: some device keeps all 20 slots.
All inputs are finite; a program needn't handle non-finite values.
Results may differ from the reference program's by a relative error of at most 0.0022.
Values may be sent and summed in bfloat16 or wider, within the bound.
No kernel may reach another device: no remote copies, remote signals or barrier semaphores. Data moves between devices by JAX's collectives and lax.ppermute only.
A program may use at most 64 MiB of HBM per device.

```python
import math
import jax
import jax.numpy as jnp
from jax import lax

MODES = 512
ALONG = 16
AROUND = 8
BLK_AXIAL = 2
BLK_CIRC = 2
PAIRS_DEV = 20
NBA = 128
NBC = 16
N_AXIAL = 64
N_CIRC = 8


def draw_pair_list(key, part):
    device_total = N_AXIAL * N_CIRC
    slot_total = PAIRS_DEV
    scores = jax.random.randint(key, (device_total, slot_total), 0, 1 << 20) * slot_total + jnp.arange(slot_total, dtype=jnp.int32)[None, :]
    ordering = jnp.argsort(scores, axis=-1, stable=True).astype(jnp.int32)
    row_block = ordering // 5
    offset_kind = ordering % 5
    along_table = jnp.array([0, 0, 1, 1, 1], jnp.int32)
    around_table = jnp.array([0, 1, -1, 0, 1], jnp.int32)
    stacked = jnp.stack([row_block, along_table[offset_kind], around_table[offset_kind]], axis=1)
    return stacked.reshape(N_AXIAL, N_CIRC, 3, slot_total).astype(jnp.int32)


def draw_pair_counts(key, part):
    device_total = N_AXIAL * N_CIRC
    count_key = jax.random.fold_in(key, 11)
    spot_key = jax.random.fold_in(key, 23)
    counts_drawn = jax.random.randint(count_key, (device_total,), PAIRS_DEV // 8, PAIRS_DEV + 1)
    fullest = jax.random.randint(spot_key, (), 0, device_total)
    counts_drawn = counts_drawn.at[fullest].set(PAIRS_DEV)
    return counts_drawn.reshape(N_AXIAL, N_CIRC).astype(jnp.int32)


def spiked(result, own_key, source, target, blocks, factor):
    owner, partner = [(jnp.arange(result.shape[position]) // (result.shape[position] // blocks)).reshape([-1 if axis == position else 1 for axis in range(result.ndim)]) for position in (source, target)]
    chosen = jax.random.permutation(own_key, blocks)[partner]
    strong = (owner == chosen) | (owner == (partner + blocks // 2) % blocks)
    return jnp.where(strong, factor * result, result)


def shard_levels(own_key, dims, pieces, low, high):
    loudness, own = 1.0, jax.random.fold_in(own_key, 6)
    for axis_at, shards_of in pieces:
        steps = jnp.exp(jax.random.uniform(jax.random.fold_in(own, axis_at), (shards_of,), jnp.float32, low / len(pieces), high / len(pieces)))
        loudness = loudness * jnp.repeat(steps, dims[axis_at] // shards_of).reshape([-1 if axis == axis_at else 1 for axis in range(len(dims))])
    return loudness


def gaussian_with(rng, shape, scale, most, pieces, heavy, kind=jnp.bfloat16):
    values = scale * jax.random.normal(rng, shape, jnp.float32)
    if pieces:
        values = values * shard_levels(rng, shape, pieces, -0.22, 0.18)
    return jnp.clip(spiked(values, jax.random.fold_in(rng, 3), *heavy), -most, most).astype(kind)


def setup_inputs(seed: int = 0) -> dict:
    key_of = jax.random.split(jax.random.key(seed), 5)
    return {
        "mode_shapes": gaussian_with(key_of[0], (NBA, NBC, ALONG * AROUND, MODES), (ALONG * AROUND * NBA * NBC) ** -0.5, 0.03125, ((0, 64), (1, 8)), (0, 3, 64, 4.0), jnp.float32),
        "amplitude": jnp.clip(jnp.exp(math.log(3.0) - 2.3025851 * jax.random.uniform(key_of[1], (NBA, NBC, ALONG * AROUND), jnp.float32) ** shard_levels(key_of[1], (NBA, NBC, ALONG * AROUND), ((0, 64), (1, 8)), -0.2, 0.2)), 0.3, 3.0),
        "pair_list": draw_pair_list(jax.random.fold_in(key_of[4], 71), 0),
        "pair_counts": draw_pair_counts(jax.random.fold_in(key_of[4], 71), 0),
    }


axial_decay = 0.125
circ_decay = 0.16
wavenumber = 0.6


def corcos_tiles(step_along, step_around, weight):
    patch_index = jnp.arange(ALONG * AROUND, dtype=jnp.int32)
    along_pos = (patch_index // AROUND).astype(jnp.float32)
    around_pos = (patch_index % AROUND).astype(jnp.float32)
    gap_along = step_along.astype(jnp.float32)[:, None, None] * ALONG + along_pos[None, None, :] - along_pos[None, :, None]
    gap_around = step_around.astype(jnp.float32)[:, None, None] * AROUND + around_pos[None, None, :] - around_pos[None, :, None]
    envelope = weight[:, None, None] * jnp.exp(-axial_decay * jnp.abs(gap_along) - circ_decay * jnp.abs(gap_around))
    real_tile = envelope * jnp.cos(wavenumber * gap_along)
    imag_tile = -envelope * jnp.sin(wavenumber * gap_along)
    return jnp.stack([real_tile, imag_tile], axis=1).astype(jnp.bfloat16)


def reference(mode_shapes, amplitude, pair_list, pair_counts):
    weighted = (mode_shapes * amplitude[..., None]).astype(jnp.bfloat16)
    widened = jnp.concatenate([weighted[:, -1:], weighted, weighted[:, :1]], axis=1)
    extended = jnp.concatenate([widened, jnp.zeros((1,) + widened.shape[1:], jnp.bfloat16)], axis=0)
    block_count = BLK_AXIAL * BLK_CIRC
    patch_count = ALONG * AROUND

    def per_device(totals, device):
        along_dev = device // N_CIRC
        around_dev = device % N_CIRC
        listing = pair_list[along_dev, around_dev]
        row_block = listing[0]
        step_along = listing[1]
        step_around = listing[2]
        slot_index = jnp.arange(PAIRS_DEV, dtype=jnp.int32)
        valid = (slot_index < pair_counts[along_dev, around_dev]).astype(jnp.float32)
        weight = valid * jnp.where((step_along == 0) & (step_around == 0), 0.5, 1.0).astype(jnp.float32)
        global_along = along_dev * BLK_AXIAL + row_block // BLK_CIRC
        global_around = around_dev * BLK_CIRC + row_block % BLK_CIRC
        columns = extended[global_along + step_along, global_around + step_around + 1]
        tiles = corcos_tiles(step_along, step_around, weight)
        products = jnp.einsum("pcij,pjm->picm", tiles.astype(jnp.float32), columns.astype(jnp.float32))
        products = products.reshape(PAIRS_DEV, patch_count, 2 * MODES)
        row_sums = jax.ops.segment_sum(products, row_block, num_segments=block_count)
        rounded = row_sums.astype(jnp.bfloat16).reshape(block_count * patch_count, 2 * MODES)
        start_along = (along_dev * BLK_AXIAL).astype(jnp.int32)
        start_around = (around_dev * BLK_CIRC).astype(jnp.int32)
        zero_index = jnp.int32(0)
        local = lax.dynamic_slice(weighted, (start_along, start_around, zero_index, zero_index), (BLK_AXIAL, BLK_CIRC, patch_count, MODES))
        local = local.reshape(block_count * patch_count, MODES)
        cross = lax.dot_general(local, rounded, (((0,), (0,)), ((), ())), preferred_element_type=jnp.float32)
        return totals + cross, None

    totals, unused = lax.scan(per_device, jnp.zeros((MODES, 2 * MODES), jnp.float32), jnp.arange(N_AXIAL * N_CIRC, dtype=jnp.int32))
    real_part = totals[:, :MODES]
    imag_part = totals[:, MODES:]
    return jnp.stack([real_part + real_part.T, imag_part - imag_part.T])
```

```python
import numpy as np
import ml_dtypes
import jax
import jax.numpy as jnp
from jax import lax
from jax.sharding import PartitionSpec as P

ALONG = 16
AROUND = 8

axial_decay = 0.125
circ_decay = 0.16
wavenumber = 0.6

OFFSETS = ((0, 0), (0, 1), (1, -1), (1, 0), (1, 1))


def base_tiles():
    patch = np.arange(ALONG * AROUND)
    along_pos = (patch // AROUND).astype(np.float32)
    around_pos = (patch % AROUND).astype(np.float32)
    tiles = []
    for oa, oc in OFFSETS:
        gap_along = np.float32(oa * ALONG) + along_pos[None, :] - along_pos[:, None]
        gap_around = np.float32(oc * AROUND) + around_pos[None, :] - around_pos[:, None]
        envelope = np.exp(
            np.float32(-axial_decay) * np.abs(gap_along) - np.float32(circ_decay) * np.abs(gap_around)
        ).astype(np.float32)
        real_tile = envelope * np.cos(np.float32(wavenumber) * gap_along).astype(np.float32)
        imag_tile = -envelope * np.sin(np.float32(wavenumber) * gap_along).astype(np.float32)
        tiles.append(np.stack([real_tile, imag_tile]))
    return np.stack(tiles).astype(ml_dtypes.bfloat16)


def shifted(block, axes, moves):
    sizes = [lax.axis_size(a) for a in axes]
    total = int(np.prod(sizes))
    pairs = []
    for dst in range(total):
        coords = list(np.unravel_index(dst, sizes))
        ok = True
        for d, (move, cyclic) in enumerate(moves):
            c = coords[d] + move
            if cyclic:
                c %= sizes[d]
            elif not 0 <= c < sizes[d]:
                ok = False
            coords[d] = c
        if ok:
            src = int(np.ravel_multi_index(coords, sizes))
            pairs.append((src, dst))
    return lax.ppermute(block, axes if len(axes) > 1 else axes[0], pairs)


def body(mode_shapes, amplitude, pair_list, pair_counts):
    along_blocks, around_blocks, patch_count, mode_count = mode_shapes.shape
    block_count = along_blocks * around_blocks
    weighted = (mode_shapes * amplitude[..., None]).astype(jnp.bfloat16)

    both = ("axial", "circ")
    right = shifted(weighted[:, 0], ("circ",), ((1, True),))
    left = shifted(weighted[1, 1], ("circ",), ((-1, True),))
    ahead = shifted(weighted[0], ("axial",), ((1, False),))
    ahead_left = shifted(weighted[0, 1], both, ((1, False), (-1, True)))
    ahead_right = shifted(weighted[0, 0], both, ((1, False), (1, True)))

    def window(x, y):
        if x < 2 and 0 <= y < 2:
            return weighted[x, y]
        if x < 2 and y == 2:
            return right[x]
        if x == 1 and y == -1:
            return left
        if x == 2 and 0 <= y < 2:
            return ahead[y]
        if x == 2 and y == -1:
            return ahead_left
        return ahead_right

    columns = jnp.stack(
        [
            jnp.concatenate([window(i + oa, j + oc) for oa, oc in OFFSETS], axis=0)
            for i in range(along_blocks)
            for j in range(around_blocks)
        ]
    )

    listing = pair_list[0, 0]
    slot_total = listing.shape[1]
    slot = jnp.arange(slot_total, dtype=jnp.int32)
    valid = (slot < pair_counts[0, 0]).astype(jnp.float32)
    half = jnp.where((listing[1] == 0) & (listing[2] == 0), 0.5, 1.0).astype(jnp.float32)
    kind = listing[1] * 3 + listing[2]
    row_hot = (listing[0][None, :] == jnp.arange(block_count)[:, None]).astype(jnp.float32)
    kind_hot = (kind[None, :] == jnp.arange(len(OFFSETS))[:, None]).astype(jnp.float32)
    weight = jnp.einsum("rs,ks,s->rk", row_hot, kind_hot, valid * half)

    tiles = jnp.asarray(base_tiles())
    lhs = (tiles.astype(jnp.float32)[None] * weight[:, :, None, None, None]).astype(jnp.bfloat16)
    lhs = jnp.transpose(lhs, (0, 2, 3, 1, 4)).reshape(block_count, 2 * patch_count, -1)
    row_sums = lax.dot_general(
        lhs, columns, (((2,), (1,)), ((0,), (0,))), preferred_element_type=jnp.float32
    )
    rounded = row_sums.astype(jnp.bfloat16).reshape(block_count, 2, patch_count, mode_count)
    rounded = jnp.transpose(rounded, (1, 0, 2, 3)).reshape(2, block_count * patch_count, mode_count)
    local = weighted.reshape(block_count * patch_count, mode_count)
    first = jnp.stack([jnp.concatenate([local, rounded[q]], axis=0) for q in range(2)])
    second = jnp.stack(
        [jnp.concatenate([rounded[0], local], axis=0), jnp.concatenate([rounded[1], -local], axis=0)]
    )
    summand = lax.dot_general(
        first, second, (((1,), (1,)), ((0,), (0,))), preferred_element_type=jnp.float32
    )
    n_ax = lax.axis_size("axial")
    n_ci = lax.axis_size("circ")
    rows = mode_count // n_ax
    cols = mode_count // n_ci
    arranged = summand.reshape(2, n_ax, rows, n_ci, cols).transpose(1, 3, 0, 2, 4)
    arranged = arranged.reshape(n_ax * n_ci, 2, rows, cols)
    result = lax.psum_scatter(arranged, both, scatter_dimension=0, tiled=True)
    return result.reshape(2, rows, cols)


def solution(mesh):
    in_specs = (
        P("axial", "circ", None, None),
        P("axial", "circ", None),
        P("axial", "circ", None, None),
        P("axial", "circ"),
    )
    out_specs = P(None, "axial", "circ")
    return jax.shard_map(body, mesh=mesh, in_specs=in_specs, out_specs=out_specs, check_vma=False)
```

```python
import numpy as np
import ml_dtypes
import jax
import jax.numpy as jnp
from jax import lax
from jax.sharding import PartitionSpec as P

ALONG = 16
AROUND = 8

axial_decay = 0.125
circ_decay = 0.16
wavenumber = 0.6

OFFSETS = ((0, 0), (0, 1), (1, -1), (1, 0), (1, 1))


def base_tiles():
    patch = np.arange(ALONG * AROUND)
    along_pos = (patch // AROUND).astype(np.float32)
    around_pos = (patch % AROUND).astype(np.float32)
    tiles = []
    for oa, oc in OFFSETS:
        gap_along = np.float32(oa * ALONG) + along_pos[None, :] - along_pos[:, None]
        gap_around = np.float32(oc * AROUND) + around_pos[None, :] - around_pos[:, None]
        envelope = np.exp(
            np.float32(-axial_decay) * np.abs(gap_along) - np.float32(circ_decay) * np.abs(gap_around)
        ).astype(np.float32)
        real_tile = envelope * np.cos(np.float32(wavenumber) * gap_along).astype(np.float32)
        imag_tile = -envelope * np.sin(np.float32(wavenumber) * gap_along).astype(np.float32)
        tiles.append(np.stack([real_tile, imag_tile]))
    return np.stack(tiles).astype(ml_dtypes.bfloat16)


def shifted(block, axes, moves):
    sizes = [lax.axis_size(a) for a in axes]
    total = int(np.prod(sizes))
    pairs = []
    for dst in range(total):
        coords = list(np.unravel_index(dst, sizes))
        ok = True
        for d, (move, cyclic) in enumerate(moves):
            c = coords[d] + move
            if cyclic:
                c %= sizes[d]
            elif not 0 <= c < sizes[d]:
                ok = False
            coords[d] = c
        if ok:
            src = int(np.ravel_multi_index(coords, sizes))
            pairs.append((src, dst))
    return lax.ppermute(block, axes if len(axes) > 1 else axes[0], pairs)


def body(mode_shapes, amplitude, pair_list, pair_counts):
    along_blocks, around_blocks, patch_count, mode_count = mode_shapes.shape
    block_count = along_blocks * around_blocks
    weighted = (mode_shapes * amplitude[..., None]).astype(jnp.bfloat16)

    both = ("axial", "circ")
    right = shifted(weighted[:, 0], ("circ",), ((1, True),))
    left = shifted(weighted[1, 1], ("circ",), ((-1, True),))
    ahead = shifted(weighted[0], ("axial",), ((1, False),))
    ahead_left = shifted(weighted[0, 1], both, ((1, False), (-1, True)))
    ahead_right = shifted(weighted[0, 0], both, ((1, False), (1, True)))

    def window(x, y):
        if x < 2 and 0 <= y < 2:
            return weighted[x, y]
        if x < 2 and y == 2:
            return right[x]
        if x == 1 and y == -1:
            return left
        if x == 2 and 0 <= y < 2:
            return ahead[y]
        if x == 2 and y == -1:
            return ahead_left
        return ahead_right

    columns = jnp.stack(
        [
            jnp.concatenate([window(i + oa, j + oc) for oa, oc in OFFSETS], axis=0)
            for i in range(along_blocks)
            for j in range(around_blocks)
        ]
    )

    listing = pair_list[0, 0]
    slot_total = listing.shape[1]
    slot = jnp.arange(slot_total, dtype=jnp.int32)
    valid = (slot < pair_counts[0, 0]).astype(jnp.float32)
    half = jnp.where((listing[1] == 0) & (listing[2] == 0), 0.5, 1.0).astype(jnp.float32)
    kind = listing[1] * 3 + listing[2]
    row_hot = (listing[0][None, :] == jnp.arange(block_count)[:, None]).astype(jnp.float32)
    kind_hot = (kind[None, :] == jnp.arange(len(OFFSETS))[:, None]).astype(jnp.float32)
    weight = jnp.einsum("rs,ks,s->rk", row_hot, kind_hot, valid * half)

    tiles = jnp.asarray(base_tiles())
    lhs = (tiles.astype(jnp.float32)[None] * weight[:, :, None, None, None]).astype(jnp.bfloat16)
    lhs = jnp.transpose(lhs, (0, 2, 3, 1, 4)).reshape(block_count, 2 * patch_count, -1)
    row_sums = lax.dot_general(
        lhs, columns, (((2,), (1,)), ((0,), (0,))), preferred_element_type=jnp.float32
    )
    rounded = row_sums.astype(jnp.bfloat16).reshape(block_count, 2, patch_count, mode_count)
    rounded = jnp.transpose(rounded, (1, 0, 2, 3)).reshape(2, block_count * patch_count, mode_count)
    local = weighted.reshape(block_count * patch_count, mode_count)
    first = jnp.stack([jnp.concatenate([local, rounded[q]], axis=0) for q in range(2)])
    second = jnp.stack(
        [jnp.concatenate([rounded[0], local], axis=0), jnp.concatenate([rounded[1], -local], axis=0)]
    )
    summand = lax.dot_general(
        first, second, (((1,), (1,)), ((0,), (0,))), preferred_element_type=jnp.float32
    )
    n_ax = lax.axis_size("axial")
    n_ci = lax.axis_size("circ")
    cols = mode_count // n_ci
    rows = mode_count // n_ax
    parts = lax.all_to_all(
        summand.reshape(2, mode_count, n_ci, cols), "circ", 2, 0, tiled=True
    )
    partial_value = parts.reshape(n_ci, 2, mode_count, cols).sum(axis=0)
    parts = lax.all_to_all(
        partial_value.reshape(2, n_ax, rows, cols), "axial", 1, 0, tiled=True
    )
    return parts.reshape(n_ax, 2, rows, cols).sum(axis=0)


def solution(mesh):
    in_specs = (
        P("axial", "circ", None, None),
        P("axial", "circ", None),
        P("axial", "circ", None, None),
        P("axial", "circ"),
    )
    out_specs = P(None, "axial", "circ")
    return jax.shard_map(body, mesh=mesh, in_specs=in_specs, out_specs=out_specs, check_vma=False)
```

```python
import numpy as np
import ml_dtypes
import jax
import jax.numpy as jnp
from jax import lax
from jax.sharding import Mesh, PartitionSpec as P

ALONG = 16
AROUND = 8

axial_decay = 0.125
circ_decay = 0.16
wavenumber = 0.6

OFFSETS = ((0, 0), (0, 1), (1, -1), (1, 0), (1, 1))


def base_tiles():
    patch = np.arange(ALONG * AROUND)
    along_pos = (patch // AROUND).astype(np.float32)
    around_pos = (patch % AROUND).astype(np.float32)
    tiles = []
    for oa, oc in OFFSETS:
        gap_along = np.float32(oa * ALONG) + along_pos[None, :] - along_pos[:, None]
        gap_around = np.float32(oc * AROUND) + around_pos[None, :] - around_pos[:, None]
        envelope = np.exp(
            np.float32(-axial_decay) * np.abs(gap_along) - np.float32(circ_decay) * np.abs(gap_around)
        ).astype(np.float32)
        real_tile = envelope * np.cos(np.float32(wavenumber) * gap_along).astype(np.float32)
        imag_tile = -envelope * np.sin(np.float32(wavenumber) * gap_along).astype(np.float32)
        tiles.append(np.stack([real_tile, imag_tile]))
    return np.stack(tiles).astype(ml_dtypes.bfloat16)


AXIAL = ("y_hi", "z", "core")
CIRC = ("x", "y_lo")


def group_size(axes):
    return int(np.prod([lax.axis_size(a) for a in axes]))


def shifted(block, axes, moves):
    sizes = [group_size(a) for a in axes]
    total = int(np.prod(sizes))
    pairs = []
    for dst in range(total):
        coords = list(np.unravel_index(dst, sizes))
        ok = True
        for d, (move, cyclic) in enumerate(moves):
            c = coords[d] + move
            if cyclic:
                c %= sizes[d]
            elif not 0 <= c < sizes[d]:
                ok = False
            coords[d] = c
        if ok:
            src = int(np.ravel_multi_index(coords, sizes))
            pairs.append((src, dst))
    return lax.ppermute(block, sum(axes, ()), pairs)


def body(mode_shapes, amplitude, pair_list, pair_counts):
    along_blocks, around_blocks, patch_count, mode_count = mode_shapes.shape
    block_count = along_blocks * around_blocks
    weighted = (mode_shapes * amplitude[..., None]).astype(jnp.bfloat16)

    both = (AXIAL, CIRC)
    right = shifted(weighted[:, 0], (CIRC,), ((1, True),))
    left = shifted(weighted[1, 1], (CIRC,), ((-1, True),))
    ahead = shifted(weighted[0], (AXIAL,), ((1, False),))
    ahead_left = shifted(weighted[0, 1], both, ((1, False), (-1, True)))
    ahead_right = shifted(weighted[0, 0], both, ((1, False), (1, True)))

    def window(x, y):
        if x < 2 and 0 <= y < 2:
            return weighted[x, y]
        if x < 2 and y == 2:
            return right[x]
        if x == 1 and y == -1:
            return left
        if x == 2 and 0 <= y < 2:
            return ahead[y]
        if x == 2 and y == -1:
            return ahead_left
        return ahead_right

    columns = jnp.stack(
        [
            jnp.concatenate([window(i + oa, j + oc) for oa, oc in OFFSETS], axis=0)
            for i in range(along_blocks)
            for j in range(around_blocks)
        ]
    )

    listing = pair_list[0, 0]
    slot_total = listing.shape[1]
    slot = jnp.arange(slot_total, dtype=jnp.int32)
    valid = (slot < pair_counts[0, 0]).astype(jnp.float32)
    half = jnp.where((listing[1] == 0) & (listing[2] == 0), 0.5, 1.0).astype(jnp.float32)
    kind = listing[1] * 3 + listing[2]
    row_hot = (listing[0][None, :] == jnp.arange(block_count)[:, None]).astype(jnp.float32)
    kind_hot = (kind[None, :] == jnp.arange(len(OFFSETS))[:, None]).astype(jnp.float32)
    weight = jnp.einsum("rs,ks,s->rk", row_hot, kind_hot, valid * half)

    tiles = jnp.asarray(base_tiles())
    lhs = (tiles.astype(jnp.float32)[None] * weight[:, :, None, None, None]).astype(jnp.bfloat16)
    lhs = jnp.transpose(lhs, (0, 2, 3, 1, 4)).reshape(block_count, 2 * patch_count, -1)
    row_sums = lax.dot_general(
        lhs, columns, (((2,), (1,)), ((0,), (0,))), preferred_element_type=jnp.float32
    )
    rounded = row_sums.astype(jnp.bfloat16).reshape(block_count, 2, patch_count, mode_count)
    rounded = jnp.transpose(rounded, (1, 0, 2, 3)).reshape(2, block_count * patch_count, mode_count)
    local = weighted.reshape(block_count * patch_count, mode_count)
    first = jnp.stack([jnp.concatenate([local, rounded[q]], axis=0) for q in range(2)])
    second = jnp.stack(
        [jnp.concatenate([rounded[0], local], axis=0), jnp.concatenate([rounded[1], -local], axis=0)]
    )
    summand = lax.dot_general(
        first, second, (((1,), (1,)), ((0,), (0,))), preferred_element_type=jnp.float32
    )
    n_core = lax.axis_size("core")
    outer = group_size(AXIAL) // n_core
    n_ci = group_size(CIRC)
    cols = mode_count // n_ci
    rows = mode_count // (outer * n_core)
    arranged = summand.reshape(2, outer, n_core, rows, n_ci, cols).transpose(4, 2, 1, 0, 3, 5)
    arranged = arranged.reshape(n_ci * n_core, outer * 2 * rows * cols)
    parts = lax.all_to_all(arranged, CIRC + ("core",), 0, 0, tiled=True)
    partial_value = parts.reshape(n_ci * n_core, outer, 2 * rows * cols).sum(axis=0)
    parts = lax.all_to_all(partial_value, AXIAL[:-1], 0, 0, tiled=True)
    return parts.sum(axis=0).reshape(2, rows, cols)


def solution(mesh):
    sizes = [mesh.shape["axial"] // 16, 8, 2, mesh.shape["circ"] // 2, 2]
    fine = Mesh(mesh.devices.reshape(sizes), AXIAL + CIRC)
    in_specs = (
        P(AXIAL, CIRC, None, None),
        P(AXIAL, CIRC, None),
        P(AXIAL, CIRC, None, None),
        P(AXIAL, CIRC),
    )
    out_specs = P(None, AXIAL, CIRC)
    return jax.shard_map(body, mesh=fine, in_specs=in_specs, out_specs=out_specs, check_vma=False)
```

```python
import numpy as np
import ml_dtypes
import jax
import jax.numpy as jnp
from jax import lax
from jax.sharding import PartitionSpec as P

ALONG = 16
AROUND = 8

axial_decay = 0.125
circ_decay = 0.16
wavenumber = 0.6

OFFSETS = ((0, 0), (0, 1), (1, -1), (1, 0), (1, 1))


def base_tiles():
    patch = np.arange(ALONG * AROUND)
    along_pos = (patch // AROUND).astype(np.float32)
    around_pos = (patch % AROUND).astype(np.float32)
    tiles = []
    for oa, oc in OFFSETS:
        gap_along = np.float32(oa * ALONG) + along_pos[None, :] - along_pos[:, None]
        gap_around = np.float32(oc * AROUND) + around_pos[None, :] - around_pos[:, None]
        envelope = np.exp(
            np.float32(-axial_decay) * np.abs(gap_along) - np.float32(circ_decay) * np.abs(gap_around)
        ).astype(np.float32)
        real_tile = envelope * np.cos(np.float32(wavenumber) * gap_along).astype(np.float32)
        imag_tile = -envelope * np.sin(np.float32(wavenumber) * gap_along).astype(np.float32)
        tiles.append(np.stack([real_tile, imag_tile]))
    return np.stack(tiles).astype(ml_dtypes.bfloat16)


def shifted(block, axes, moves):
    sizes = [lax.axis_size(a) for a in axes]
    total = int(np.prod(sizes))
    pairs = []
    for dst in range(total):
        coords = list(np.unravel_index(dst, sizes))
        ok = True
        for d, (move, cyclic) in enumerate(moves):
            c = coords[d] + move
            if cyclic:
                c %= sizes[d]
            elif not 0 <= c < sizes[d]:
                ok = False
            coords[d] = c
        if ok:
            src = int(np.ravel_multi_index(coords, sizes))
            pairs.append((src, dst))
    return lax.ppermute(block, axes if len(axes) > 1 else axes[0], pairs)


def body(mode_shapes, amplitude, pair_list, pair_counts):
    along_blocks, around_blocks, patch_count, mode_count = mode_shapes.shape
    block_count = along_blocks * around_blocks
    weighted = (mode_shapes * amplitude[..., None]).astype(jnp.bfloat16)

    both = ("axial", "circ")
    right = shifted(weighted[:, 0], ("circ",), ((1, True),))
    left = shifted(weighted[1, 1], ("circ",), ((-1, True),))
    ahead = shifted(weighted[0], ("axial",), ((1, False),))
    ahead_left = shifted(weighted[0, 1], both, ((1, False), (-1, True)))
    ahead_right = shifted(weighted[0, 0], both, ((1, False), (1, True)))

    def window(x, y):
        if x < 2 and 0 <= y < 2:
            return weighted[x, y]
        if x < 2 and y == 2:
            return right[x]
        if x == 1 and y == -1:
            return left
        if x == 2 and 0 <= y < 2:
            return ahead[y]
        if x == 2 and y == -1:
            return ahead_left
        return ahead_right

    columns = jnp.stack(
        [
            jnp.concatenate([window(i + oa, j + oc) for oa, oc in OFFSETS], axis=0)
            for i in range(along_blocks)
            for j in range(around_blocks)
        ]
    )

    listing = pair_list[0, 0]
    slot_total = listing.shape[1]
    slot = jnp.arange(slot_total, dtype=jnp.int32)
    valid = (slot < pair_counts[0, 0]).astype(jnp.float32)
    half = jnp.where((listing[1] == 0) & (listing[2] == 0), 0.5, 1.0).astype(jnp.float32)
    kind = listing[1] * 3 + listing[2]
    row_hot = (listing[0][None, :] == jnp.arange(block_count)[:, None]).astype(jnp.float32)
    kind_hot = (kind[None, :] == jnp.arange(len(OFFSETS))[:, None]).astype(jnp.float32)
    weight = jnp.einsum("rs,ks,s->rk", row_hot, kind_hot, valid * half)

    tiles = jnp.asarray(base_tiles())
    lhs = (tiles.astype(jnp.float32)[None] * weight[:, :, None, None, None]).astype(jnp.bfloat16)
    lhs = jnp.transpose(lhs, (0, 2, 3, 1, 4)).reshape(block_count, 2 * patch_count, -1)
    row_sums = lax.dot_general(
        lhs, columns, (((2,), (1,)), ((0,), (0,))), preferred_element_type=jnp.float32
    )
    rounded = row_sums.astype(jnp.bfloat16).reshape(block_count, 2, patch_count, mode_count)
    rounded = jnp.transpose(rounded, (1, 0, 2, 3)).reshape(2, block_count * patch_count, mode_count)
    local = weighted.reshape(block_count * patch_count, mode_count)
    first = [jnp.concatenate([local, rounded[q]], axis=0) for q in range(2)]
    second = [jnp.concatenate([rounded[0], local], axis=0), jnp.concatenate([rounded[1], -local], axis=0)]
    flipped = jnp.stack(
        [
            lax.dot_general(second[q], first[q], (((0,), (0,)), ((), ())), preferred_element_type=jnp.float32)
            for q in range(2)
        ],
        axis=1,
    )
    n_ax = lax.axis_size("axial")
    n_ci = lax.axis_size("circ")
    cols = mode_count // n_ci
    rows = mode_count // n_ax
    parts = lax.all_to_all(flipped.reshape(n_ci, cols * 2 * mode_count), "circ", 0, 0, tiled=True)
    partial_value = parts.reshape(n_ci, cols, 2, n_ax, rows).sum(axis=0)
    arranged = partial_value.transpose(2, 1, 3, 0).reshape(n_ax, 2 * rows * cols)
    parts = lax.all_to_all(arranged, "axial", 0, 0, tiled=True)
    return parts.sum(axis=0).reshape(2, rows, cols)


def solution(mesh):
    in_specs = (
        P("axial", "circ", None, None),
        P("axial", "circ", None),
        P("axial", "circ", None, None),
        P("axial", "circ"),
    )
    out_specs = P(None, "axial", "circ")
    return jax.shard_map(body, mesh=mesh, in_specs=in_specs, out_specs=out_specs, check_vma=False)
```

```python
import numpy as np
import ml_dtypes
import jax
import jax.numpy as jnp
from jax import lax
from jax.sharding import Mesh, PartitionSpec as P

ALONG = 16
AROUND = 8

axial_decay = 0.125
circ_decay = 0.16
wavenumber = 0.6

OFFSETS = ((0, 0), (0, 1), (1, -1), (1, 0), (1, 1))


def base_tiles():
    patch = np.arange(ALONG * AROUND)
    along_pos = (patch // AROUND).astype(np.float32)
    around_pos = (patch % AROUND).astype(np.float32)
    tiles = []
    for oa, oc in OFFSETS:
        gap_along = np.float32(oa * ALONG) + along_pos[None, :] - along_pos[:, None]
        gap_around = np.float32(oc * AROUND) + around_pos[None, :] - around_pos[:, None]
        envelope = np.exp(
            np.float32(-axial_decay) * np.abs(gap_along) - np.float32(circ_decay) * np.abs(gap_around)
        ).astype(np.float32)
        real_tile = envelope * np.cos(np.float32(wavenumber) * gap_along).astype(np.float32)
        imag_tile = -envelope * np.sin(np.float32(wavenumber) * gap_along).astype(np.float32)
        tiles.append(np.stack([real_tile, imag_tile]))
    return np.stack(tiles).astype(ml_dtypes.bfloat16)


AXIAL = ("y_hi", "z", "core")
CIRC = ("x", "y_lo")


def group_size(axes):
    return int(np.prod([lax.axis_size(a) for a in axes]))


def shifted(block, axes, moves):
    sizes = [group_size(a) for a in axes]
    total = int(np.prod(sizes))
    pairs = []
    for dst in range(total):
        coords = list(np.unravel_index(dst, sizes))
        ok = True
        for d, (move, cyclic) in enumerate(moves):
            c = coords[d] + move
            if cyclic:
                c %= sizes[d]
            elif not 0 <= c < sizes[d]:
                ok = False
            coords[d] = c
        if ok:
            src = int(np.ravel_multi_index(coords, sizes))
            pairs.append((src, dst))
    return lax.ppermute(block, sum(axes, ()), pairs)


def body(mode_shapes, amplitude, pair_list, pair_counts):
    along_blocks, around_blocks, patch_count, mode_count = mode_shapes.shape
    block_count = along_blocks * around_blocks
    weighted = (mode_shapes * amplitude[..., None]).astype(jnp.bfloat16)

    both = (AXIAL, CIRC)
    right = shifted(weighted[:, 0], (CIRC,), ((1, True),))
    left = shifted(weighted[1, 1], (CIRC,), ((-1, True),))
    ahead = shifted(weighted[0], (AXIAL,), ((1, False),))
    ahead_left = shifted(weighted[0, 1], both, ((1, False), (-1, True)))
    ahead_right = shifted(weighted[0, 0], both, ((1, False), (1, True)))

    def window(x, y):
        if x < 2 and 0 <= y < 2:
            return weighted[x, y]
        if x < 2 and y == 2:
            return right[x]
        if x == 1 and y == -1:
            return left
        if x == 2 and 0 <= y < 2:
            return ahead[y]
        if x == 2 and y == -1:
            return ahead_left
        return ahead_right

    columns = jnp.stack(
        [
            jnp.concatenate([window(i + oa, j + oc) for oa, oc in OFFSETS], axis=0)
            for i in range(along_blocks)
            for j in range(around_blocks)
        ]
    )

    listing = pair_list[0, 0]
    slot_total = listing.shape[1]
    slot = jnp.arange(slot_total, dtype=jnp.int32)
    valid = (slot < pair_counts[0, 0]).astype(jnp.float32)
    half = jnp.where((listing[1] == 0) & (listing[2] == 0), 0.5, 1.0).astype(jnp.float32)
    kind = listing[1] * 3 + listing[2]
    row_hot = (listing[0][None, :] == jnp.arange(block_count)[:, None]).astype(jnp.float32)
    kind_hot = (kind[None, :] == jnp.arange(len(OFFSETS))[:, None]).astype(jnp.float32)
    weight = jnp.einsum("rs,ks,s->rk", row_hot, kind_hot, valid * half)

    tiles = jnp.asarray(base_tiles())
    lhs = (tiles.astype(jnp.float32)[None] * weight[:, :, None, None, None]).astype(jnp.bfloat16)
    lhs = jnp.transpose(lhs, (0, 2, 3, 1, 4)).reshape(block_count, 2 * patch_count, -1)
    row_sums = lax.dot_general(
        lhs, columns, (((2,), (1,)), ((0,), (0,))), preferred_element_type=jnp.float32
    )
    rounded = row_sums.astype(jnp.bfloat16).reshape(block_count, 2, patch_count, mode_count)
    rounded = jnp.transpose(rounded, (1, 0, 2, 3)).reshape(2, block_count * patch_count, mode_count)
    local = weighted.reshape(block_count * patch_count, mode_count)
    n_core = lax.axis_size("core")
    outer = group_size(AXIAL) // n_core
    n_ci = group_size(CIRC)
    cols = mode_count // n_ci
    rows = mode_count // (outer * n_core)
    first = jnp.concatenate([local, rounded[0], rounded[1]], axis=0)
    first = first.reshape(-1, outer, n_core, rows).transpose(0, 2, 1, 3).reshape(first.shape[0], mode_count)
    zeros = jnp.zeros_like(local)
    second = jnp.concatenate(
        [
            jnp.concatenate([rounded[0], local, zeros], axis=0),
            jnp.concatenate([rounded[1], zeros, -local], axis=0),
        ],
        axis=1,
    )
    summand = lax.dot_general(
        first, second, (((0,), (0,)), ((), ())), preferred_element_type=jnp.float32
    )
    parts = lax.all_to_all(summand.reshape(n_core, -1), "core", 0, 0, tiled=True)
    halves = parts.reshape(n_core, outer, rows, 2, n_ci, cols).sum(axis=0)
    arranged = halves.transpose(3, 0, 2, 1, 4).reshape(n_ci, -1)
    parts = lax.all_to_all(arranged, CIRC, 0, 0, tiled=True)
    partial_value = parts.reshape(n_ci, outer, -1).sum(axis=0)
    parts = lax.all_to_all(partial_value, AXIAL[:-1], 0, 0, tiled=True)
    return parts.sum(axis=0).reshape(2, rows, cols)


def solution(mesh):
    sizes = [mesh.shape["axial"] // 16, 8, 2, mesh.shape["circ"] // 2, 2]
    fine = Mesh(mesh.devices.reshape(sizes), AXIAL + CIRC)
    in_specs = (
        P(AXIAL, CIRC, None, None),
        P(AXIAL, CIRC, None),
        P(AXIAL, CIRC, None, None),
        P(AXIAL, CIRC),
    )
    out_specs = P(None, AXIAL, CIRC)
    return jax.shard_map(body, mesh=fine, in_specs=in_specs, out_specs=out_specs, check_vma=False)
```

```python
import numpy as np
import ml_dtypes
import jax
import jax.numpy as jnp
from jax import lax
from jax.sharding import PartitionSpec as P

ALONG = 16
AROUND = 8

axial_decay = 0.125
circ_decay = 0.16
wavenumber = 0.6

OFFSETS = ((0, 0), (0, 1), (1, -1), (1, 0), (1, 1))


def base_tiles():
    patch = np.arange(ALONG * AROUND)
    along_pos = (patch // AROUND).astype(np.float32)
    around_pos = (patch % AROUND).astype(np.float32)
    tiles = []
    for oa, oc in OFFSETS:
        gap_along = np.float32(oa * ALONG) + along_pos[None, :] - along_pos[:, None]
        gap_around = np.float32(oc * AROUND) + around_pos[None, :] - around_pos[:, None]
        envelope = np.exp(
            np.float32(-axial_decay) * np.abs(gap_along) - np.float32(circ_decay) * np.abs(gap_around)
        ).astype(np.float32)
        real_tile = envelope * np.cos(np.float32(wavenumber) * gap_along).astype(np.float32)
        imag_tile = -envelope * np.sin(np.float32(wavenumber) * gap_along).astype(np.float32)
        tiles.append(np.stack([real_tile, imag_tile]))
    return np.stack(tiles).astype(ml_dtypes.bfloat16)


def shifted(block, axes, moves):
    sizes = [lax.axis_size(a) for a in axes]
    total = int(np.prod(sizes))
    pairs = []
    for dst in range(total):
        coords = list(np.unravel_index(dst, sizes))
        ok = True
        for d, (move, cyclic) in enumerate(moves):
            c = coords[d] + move
            if cyclic:
                c %= sizes[d]
            elif not 0 <= c < sizes[d]:
                ok = False
            coords[d] = c
        if ok:
            src = int(np.ravel_multi_index(coords, sizes))
            pairs.append((src, dst))
    return lax.ppermute(block, axes if len(axes) > 1 else axes[0], pairs)


def body(mode_shapes, amplitude, pair_list, pair_counts):
    along_blocks, around_blocks, patch_count, mode_count = mode_shapes.shape
    block_count = along_blocks * around_blocks
    weighted = (mode_shapes * amplitude[..., None]).astype(jnp.bfloat16)

    both = ("axial", "circ")
    right = shifted(weighted[:, 0], ("circ",), ((1, True),))
    left = shifted(weighted[:, 1], ("circ",), ((-1, True),))
    widened = jnp.stack([left[0], weighted[0, 0], weighted[0, 1], right[0]])
    ahead = shifted(widened, ("axial",), ((1, False),))

    def window(x, y):
        if x < 2 and 0 <= y < 2:
            return weighted[x, y]
        if x < 2 and y == 2:
            return right[x]
        if x < 2 and y == -1:
            return left[x]
        return ahead[y + 1]

    columns = jnp.stack(
        [
            jnp.concatenate([window(i + oa, j + oc) for oa, oc in OFFSETS], axis=0)
            for i in range(along_blocks)
            for j in range(around_blocks)
        ]
    )

    listing = pair_list[0, 0]
    slot_total = listing.shape[1]
    slot = jnp.arange(slot_total, dtype=jnp.int32)
    valid = (slot < pair_counts[0, 0]).astype(jnp.float32)
    half = jnp.where((listing[1] == 0) & (listing[2] == 0), 0.5, 1.0).astype(jnp.float32)
    kind = listing[1] * 3 + listing[2]
    row_hot = (listing[0][None, :] == jnp.arange(block_count)[:, None]).astype(jnp.float32)
    kind_hot = (kind[None, :] == jnp.arange(len(OFFSETS))[:, None]).astype(jnp.float32)
    weight = jnp.einsum("rs,ks,s->rk", row_hot, kind_hot, valid * half)

    tiles = jnp.asarray(base_tiles())
    lhs = (tiles.astype(jnp.float32)[None] * weight[:, :, None, None, None]).astype(jnp.bfloat16)
    lhs = jnp.transpose(lhs, (0, 2, 3, 1, 4)).reshape(block_count, 2 * patch_count, -1)
    row_sums = lax.dot_general(
        lhs, columns, (((2,), (1,)), ((0,), (0,))), preferred_element_type=jnp.float32
    )
    rounded = row_sums.astype(jnp.bfloat16).reshape(block_count, 2, patch_count, mode_count)
    rounded = jnp.transpose(rounded, (1, 0, 2, 3)).reshape(2, block_count * patch_count, mode_count)
    local = weighted.reshape(block_count * patch_count, mode_count)
    first = jnp.stack([jnp.concatenate([local, rounded[q]], axis=0) for q in range(2)])
    second = jnp.stack(
        [jnp.concatenate([rounded[0], local], axis=0), jnp.concatenate([rounded[1], -local], axis=0)]
    )
    summand = lax.dot_general(
        first, second, (((1,), (1,)), ((0,), (0,))), preferred_element_type=jnp.float32
    )
    n_ax = lax.axis_size("axial")
    n_ci = lax.axis_size("circ")
    cols = mode_count // n_ci
    rows = mode_count // n_ax
    parts = lax.all_to_all(
        summand.reshape(2, mode_count, n_ci, cols), "circ", 2, 0, tiled=True
    )
    partial_value = parts.reshape(n_ci, 2, mode_count, cols).sum(axis=0)
    parts = lax.all_to_all(
        partial_value.reshape(2, n_ax, rows, cols), "axial", 1, 0, tiled=True
    )
    return parts.reshape(n_ax, 2, rows, cols).sum(axis=0)


def solution(mesh):
    in_specs = (
        P("axial", "circ", None, None),
        P("axial", "circ", None),
        P("axial", "circ", None, None),
        P("axial", "circ"),
    )
    out_specs = P(None, "axial", "circ")
    return jax.shard_map(body, mesh=mesh, in_specs=in_specs, out_specs=out_specs, check_vma=False)
```

```python
import numpy as np
import ml_dtypes
import jax
import jax.numpy as jnp
from jax import lax
from jax.sharding import PartitionSpec as P

ALONG = 16
AROUND = 8

axial_decay = 0.125
circ_decay = 0.16
wavenumber = 0.6

OFFSETS = ((0, 0), (0, 1), (1, -1), (1, 0), (1, 1))


def base_tiles():
    patch = np.arange(ALONG * AROUND)
    along_pos = (patch // AROUND).astype(np.float32)
    around_pos = (patch % AROUND).astype(np.float32)
    tiles = []
    for oa, oc in OFFSETS:
        gap_along = np.float32(oa * ALONG) + along_pos[None, :] - along_pos[:, None]
        gap_around = np.float32(oc * AROUND) + around_pos[None, :] - around_pos[:, None]
        envelope = np.exp(
            np.float32(-axial_decay) * np.abs(gap_along) - np.float32(circ_decay) * np.abs(gap_around)
        ).astype(np.float32)
        real_tile = envelope * np.cos(np.float32(wavenumber) * gap_along).astype(np.float32)
        imag_tile = -envelope * np.sin(np.float32(wavenumber) * gap_along).astype(np.float32)
        tiles.append(np.stack([real_tile, imag_tile]))
    return np.stack(tiles).astype(ml_dtypes.bfloat16)


def shifted(block, axes, moves):
    sizes = [lax.axis_size(a) for a in axes]
    total = int(np.prod(sizes))
    pairs = []
    for dst in range(total):
        coords = list(np.unravel_index(dst, sizes))
        ok = True
        for d, (move, cyclic) in enumerate(moves):
            c = coords[d] + move
            if cyclic:
                c %= sizes[d]
            elif not 0 <= c < sizes[d]:
                ok = False
            coords[d] = c
        if ok:
            src = int(np.ravel_multi_index(coords, sizes))
            pairs.append((src, dst))
    return lax.ppermute(block, axes if len(axes) > 1 else axes[0], pairs)


def body(mode_shapes, amplitude, pair_list, pair_counts):
    along_blocks, around_blocks, patch_count, mode_count = mode_shapes.shape
    block_count = along_blocks * around_blocks
    weighted = (mode_shapes * amplitude[..., None]).astype(jnp.bfloat16)

    both = ("axial", "circ")
    right = shifted(weighted[:, 0], ("circ",), ((1, True),))
    left = shifted(weighted[1, 1], ("circ",), ((-1, True),))
    ahead = shifted(weighted[0], ("axial",), ((1, False),))
    ahead_left = shifted(weighted[0, 1], both, ((1, False), (-1, True)))
    ahead_right = shifted(weighted[0, 0], both, ((1, False), (1, True)))

    def window(x, y):
        if x < 2 and 0 <= y < 2:
            return weighted[x, y]
        if x < 2 and y == 2:
            return right[x]
        if x == 1 and y == -1:
            return left
        if x == 2 and 0 <= y < 2:
            return ahead[y]
        if x == 2 and y == -1:
            return ahead_left
        return ahead_right

    columns = jnp.stack(
        [
            jnp.concatenate([window(i + oa, j + oc) for oa, oc in OFFSETS], axis=0)
            for i in range(along_blocks)
            for j in range(around_blocks)
        ]
    )

    listing = pair_list[0, 0]
    slot_total = listing.shape[1]
    slot = jnp.arange(slot_total, dtype=jnp.int32)
    valid = (slot < pair_counts[0, 0]).astype(jnp.float32)
    half = jnp.where((listing[1] == 0) & (listing[2] == 0), 0.5, 1.0).astype(jnp.float32)
    kind = listing[1] * 3 + listing[2]
    row_hot = (listing[0][None, :] == jnp.arange(block_count)[:, None]).astype(jnp.float32)
    kind_hot = (kind[None, :] == jnp.arange(len(OFFSETS))[:, None]).astype(jnp.float32)
    weight = jnp.einsum("rs,ks,s->rk", row_hot, kind_hot, valid * half)

    tiles = jnp.asarray(base_tiles())
    lhs = (tiles.astype(jnp.float32)[None] * weight[:, :, None, None, None]).astype(jnp.bfloat16)
    lhs = jnp.transpose(lhs, (0, 2, 3, 1, 4)).reshape(block_count, 2 * patch_count, -1)
    row_sums = lax.dot_general(
        lhs, columns, (((2,), (1,)), ((0,), (0,))), preferred_element_type=jnp.float32
    )
    rounded = row_sums.astype(jnp.bfloat16).reshape(block_count, 2, patch_count, mode_count)
    rounded = jnp.transpose(rounded, (1, 0, 2, 3)).reshape(2, block_count * patch_count, mode_count)
    local = weighted.reshape(block_count * patch_count, mode_count)
    first = jnp.stack([jnp.concatenate([local, rounded[q]], axis=0) for q in range(2)])
    second = jnp.stack(
        [jnp.concatenate([rounded[0], local], axis=0), jnp.concatenate([rounded[1], -local], axis=0)]
    )
    summand = lax.dot_general(
        first, second, (((1,), (1,)), ((0,), (0,))), preferred_element_type=jnp.float32
    )
    n_ax = lax.axis_size("axial")
    n_ci = lax.axis_size("circ")
    cols = mode_count // n_ci
    rows = mode_count // n_ax
    parts = lax.all_to_all(
        summand.reshape(2, mode_count, n_ci, cols), "circ", 2, 0, tiled=True
    )
    partial_value = parts.reshape(n_ci, 2, mode_count, cols).sum(axis=0)
    arranged = partial_value.reshape(2, n_ax, rows, cols).transpose(1, 0, 2, 3)
    arranged = arranged.reshape(n_ax, 2 * rows * cols // 128, 128)
    parts = lax.all_to_all(arranged, "axial", 0, 0, tiled=True)
    return parts.sum(axis=0).reshape(2, rows, cols)


def solution(mesh):
    in_specs = (
        P("axial", "circ", None, None),
        P("axial", "circ", None),
        P("axial", "circ", None, None),
        P("axial", "circ"),
    )
    out_specs = P(None, "axial", "circ")
    return jax.shard_map(body, mesh=mesh, in_specs=in_specs, out_specs=out_specs, check_vma=False)
```

```python
import numpy as np
import ml_dtypes
import jax
import jax.numpy as jnp
from jax import lax
from jax.sharding import Mesh, PartitionSpec as P

ALONG = 16
AROUND = 8

axial_decay = 0.125
circ_decay = 0.16
wavenumber = 0.6

OFFSETS = ((0, 0), (0, 1), (1, -1), (1, 0), (1, 1))


def base_tiles():
    patch = np.arange(ALONG * AROUND)
    along_pos = (patch // AROUND).astype(np.float32)
    around_pos = (patch % AROUND).astype(np.float32)
    tiles = []
    for oa, oc in OFFSETS:
        gap_along = np.float32(oa * ALONG) + along_pos[None, :] - along_pos[:, None]
        gap_around = np.float32(oc * AROUND) + around_pos[None, :] - around_pos[:, None]
        envelope = np.exp(
            np.float32(-axial_decay) * np.abs(gap_along) - np.float32(circ_decay) * np.abs(gap_around)
        ).astype(np.float32)
        real_tile = envelope * np.cos(np.float32(wavenumber) * gap_along).astype(np.float32)
        imag_tile = -envelope * np.sin(np.float32(wavenumber) * gap_along).astype(np.float32)
        tiles.append(np.stack([real_tile, imag_tile]))
    return np.stack(tiles).astype(ml_dtypes.bfloat16)


AXIAL = ("y_hi", "z", "core")
CIRC = ("x", "y_lo")


def group_size(axes):
    return int(np.prod([lax.axis_size(a) for a in axes]))


def shifted(block, axes, moves):
    sizes = [group_size(a) for a in axes]
    total = int(np.prod(sizes))
    pairs = []
    for dst in range(total):
        coords = list(np.unravel_index(dst, sizes))
        ok = True
        for d, (move, cyclic) in enumerate(moves):
            c = coords[d] + move
            if cyclic:
                c %= sizes[d]
            elif not 0 <= c < sizes[d]:
                ok = False
            coords[d] = c
        if ok:
            src = int(np.ravel_multi_index(coords, sizes))
            pairs.append((src, dst))
    return lax.ppermute(block, sum(axes, ()), pairs)


def body(mode_shapes, amplitude, pair_list, pair_counts):
    along_blocks, around_blocks, patch_count, mode_count = mode_shapes.shape
    block_count = along_blocks * around_blocks
    weighted = (mode_shapes * amplitude[..., None]).astype(jnp.bfloat16)

    both = (AXIAL, CIRC)
    right = shifted(weighted[:, 0], (CIRC,), ((1, True),))
    left = shifted(weighted[1, 1], (CIRC,), ((-1, True),))
    ahead = shifted(weighted[0], (AXIAL,), ((1, False),))
    ahead_left = shifted(weighted[0, 1], both, ((1, False), (-1, True)))
    ahead_right = shifted(weighted[0, 0], both, ((1, False), (1, True)))

    def window(x, y):
        if x < 2 and 0 <= y < 2:
            return weighted[x, y]
        if x < 2 and y == 2:
            return right[x]
        if x == 1 and y == -1:
            return left
        if x == 2 and 0 <= y < 2:
            return ahead[y]
        if x == 2 and y == -1:
            return ahead_left
        return ahead_right

    columns = jnp.stack(
        [
            jnp.concatenate([window(i + oa, j + oc) for oa, oc in OFFSETS], axis=0)
            for i in range(along_blocks)
            for j in range(around_blocks)
        ]
    )

    listing = pair_list[0, 0]
    slot_total = listing.shape[1]
    slot = jnp.arange(slot_total, dtype=jnp.int32)
    valid = (slot < pair_counts[0, 0]).astype(jnp.float32)
    half = jnp.where((listing[1] == 0) & (listing[2] == 0), 0.5, 1.0).astype(jnp.float32)
    kind = listing[1] * 3 + listing[2]
    row_hot = (listing[0][None, :] == jnp.arange(block_count)[:, None]).astype(jnp.float32)
    kind_hot = (kind[None, :] == jnp.arange(len(OFFSETS))[:, None]).astype(jnp.float32)
    weight = jnp.einsum("rs,ks,s->rk", row_hot, kind_hot, valid * half)

    tiles = jnp.asarray(base_tiles())
    lhs = (tiles.astype(jnp.float32)[None] * weight[:, :, None, None, None]).astype(jnp.bfloat16)
    lhs = jnp.transpose(lhs, (0, 2, 3, 1, 4)).reshape(block_count, 2 * patch_count, -1)
    row_sums = lax.dot_general(
        lhs, columns, (((2,), (1,)), ((0,), (0,))), preferred_element_type=jnp.float32
    )
    rounded = row_sums.astype(jnp.bfloat16).reshape(block_count, 2, patch_count, mode_count)
    rounded = jnp.transpose(rounded, (1, 0, 2, 3)).reshape(2, block_count * patch_count, mode_count)
    local = weighted.reshape(block_count * patch_count, mode_count)
    first = jnp.stack([jnp.concatenate([local, rounded[q]], axis=0) for q in range(2)])
    second = jnp.stack(
        [jnp.concatenate([rounded[0], local], axis=0), jnp.concatenate([rounded[1], -local], axis=0)]
    )
    summand = lax.dot_general(
        first, second, (((1,), (1,)), ((0,), (0,))), preferred_element_type=jnp.float32
    )
    n_core = lax.axis_size("core")
    outer = group_size(AXIAL) // n_core
    n_ci = group_size(CIRC)
    cols = mode_count // n_ci
    rows = mode_count // (outer * n_core)
    split = summand.reshape(2, outer, n_core, rows, mode_count)
    mine = lax.axis_index("core")
    keep = lax.dynamic_index_in_dim(split, mine, axis=2, keepdims=False)
    send = lax.dynamic_index_in_dim(split, n_core - 1 - mine, axis=2, keepdims=False)
    pairs = [(k, n_core - 1 - k) for k in range(n_core)]
    half = keep + lax.ppermute(send, "core", pairs)
    parts = lax.all_to_all(half.reshape(2, outer, rows, n_ci, cols), CIRC, 3, 0, tiled=True)
    partial_value = parts.reshape(n_ci, 2, outer, rows, cols).sum(axis=0)
    arranged = partial_value.transpose(1, 0, 2, 3).reshape(outer, 2 * rows * cols // 128, 128)
    parts = lax.all_to_all(arranged, AXIAL[:-1], 0, 0, tiled=True)
    return parts.sum(axis=0).reshape(2, rows, cols)


def solution(mesh):
    sizes = [mesh.shape["axial"] // 16, 8, 2, mesh.shape["circ"] // 2, 2]
    fine = Mesh(mesh.devices.reshape(sizes), AXIAL + CIRC)
    in_specs = (
        P(AXIAL, CIRC, None, None),
        P(AXIAL, CIRC, None),
        P(AXIAL, CIRC, None, None),
        P(AXIAL, CIRC),
    )
    out_specs = P(None, AXIAL, CIRC)
    return jax.shard_map(body, mesh=fine, in_specs=in_specs, out_specs=out_specs, check_vma=False)
```

```python
import numpy as np
import ml_dtypes
import jax
import jax.numpy as jnp
from jax import lax
from jax.sharding import Mesh, PartitionSpec as P

ALONG = 16
AROUND = 8

axial_decay = 0.125
circ_decay = 0.16
wavenumber = 0.6

OFFSETS = ((0, 0), (0, 1), (1, -1), (1, 0), (1, 1))


def base_tiles():
    patch = np.arange(ALONG * AROUND)
    along_pos = (patch // AROUND).astype(np.float32)
    around_pos = (patch % AROUND).astype(np.float32)
    tiles = []
    for oa, oc in OFFSETS:
        gap_along = np.float32(oa * ALONG) + along_pos[None, :] - along_pos[:, None]
        gap_around = np.float32(oc * AROUND) + around_pos[None, :] - around_pos[:, None]
        envelope = np.exp(
            np.float32(-axial_decay) * np.abs(gap_along) - np.float32(circ_decay) * np.abs(gap_around)
        ).astype(np.float32)
        real_tile = envelope * np.cos(np.float32(wavenumber) * gap_along).astype(np.float32)
        imag_tile = -envelope * np.sin(np.float32(wavenumber) * gap_along).astype(np.float32)
        tiles.append(np.stack([real_tile, imag_tile]))
    return np.stack(tiles).astype(ml_dtypes.bfloat16)


AXIAL = ("y_hi", "z", "core")
CIRC = ("x", "y_lo")


def group_size(axes):
    return int(np.prod([lax.axis_size(a) for a in axes]))


def shifted(block, axes, moves):
    sizes = [group_size(a) for a in axes]
    total = int(np.prod(sizes))
    pairs = []
    for dst in range(total):
        coords = list(np.unravel_index(dst, sizes))
        ok = True
        for d, (move, cyclic) in enumerate(moves):
            c = coords[d] + move
            if cyclic:
                c %= sizes[d]
            elif not 0 <= c < sizes[d]:
                ok = False
            coords[d] = c
        if ok:
            src = int(np.ravel_multi_index(coords, sizes))
            pairs.append((src, dst))
    return lax.ppermute(block, sum(axes, ()), pairs)


def body(mode_shapes, amplitude, pair_list, pair_counts):
    along_blocks, around_blocks, patch_count, mode_count = mode_shapes.shape
    block_count = along_blocks * around_blocks
    weighted = (mode_shapes * amplitude[..., None]).astype(jnp.bfloat16)

    both = (AXIAL, CIRC)
    right = shifted(weighted[:, 0], (CIRC,), ((1, True),))
    left = shifted(weighted[1, 1], (CIRC,), ((-1, True),))
    ahead = shifted(weighted[0], (AXIAL,), ((1, False),))
    ahead_left = shifted(weighted[0, 1], both, ((1, False), (-1, True)))
    ahead_right = shifted(weighted[0, 0], both, ((1, False), (1, True)))

    def window(x, y):
        if x < 2 and 0 <= y < 2:
            return weighted[x, y]
        if x < 2 and y == 2:
            return right[x]
        if x == 1 and y == -1:
            return left
        if x == 2 and 0 <= y < 2:
            return ahead[y]
        if x == 2 and y == -1:
            return ahead_left
        return ahead_right

    columns = jnp.stack(
        [
            jnp.concatenate([window(i + oa, j + oc) for oa, oc in OFFSETS], axis=0)
            for i in range(along_blocks)
            for j in range(around_blocks)
        ]
    )

    listing = pair_list[0, 0]
    slot_total = listing.shape[1]
    slot = jnp.arange(slot_total, dtype=jnp.int32)
    valid = (slot < pair_counts[0, 0]).astype(jnp.float32)
    half = jnp.where((listing[1] == 0) & (listing[2] == 0), 0.5, 1.0).astype(jnp.float32)
    kind = listing[1] * 3 + listing[2]
    row_hot = (listing[0][None, :] == jnp.arange(block_count)[:, None]).astype(jnp.float32)
    kind_hot = (kind[None, :] == jnp.arange(len(OFFSETS))[:, None]).astype(jnp.float32)
    weight = jnp.einsum("rs,ks,s->rk", row_hot, kind_hot, valid * half)

    tiles = jnp.asarray(base_tiles())
    lhs = (tiles.astype(jnp.float32)[None] * weight[:, :, None, None, None]).astype(jnp.bfloat16)
    lhs = jnp.transpose(lhs, (0, 2, 3, 1, 4)).reshape(block_count, 2 * patch_count, -1)
    row_sums = lax.dot_general(
        lhs, columns, (((2,), (1,)), ((0,), (0,))), preferred_element_type=jnp.float32
    )
    rounded = row_sums.astype(jnp.bfloat16).reshape(block_count, 2, patch_count, mode_count)
    rounded = jnp.transpose(rounded, (1, 0, 2, 3)).reshape(2, block_count * patch_count, mode_count)
    local = weighted.reshape(block_count * patch_count, mode_count)
    first = jnp.stack([jnp.concatenate([local, rounded[q]], axis=0) for q in range(2)])
    second = jnp.stack(
        [jnp.concatenate([rounded[0], local], axis=0), jnp.concatenate([rounded[1], -local], axis=0)]
    )
    summand = lax.dot_general(
        first, second, (((1,), (1,)), ((0,), (0,))), preferred_element_type=jnp.float32
    )
    n_core = lax.axis_size("core")
    outer = group_size(AXIAL) // n_core
    n_ci = group_size(CIRC)
    cols = mode_count // n_ci
    rows = mode_count // (outer * n_core)
    split = summand.reshape(2, outer, n_core, rows, mode_count)
    mine = lax.axis_index("core")
    keep = lax.dynamic_index_in_dim(split, mine, axis=2, keepdims=False)
    send = lax.dynamic_index_in_dim(split, n_core - 1 - mine, axis=2, keepdims=False)
    pairs = [(k, n_core - 1 - k) for k in range(n_core)]
    half = keep + lax.ppermute(send, "core", pairs)
    arranged = half.reshape(2, outer, rows, n_ci, cols).transpose(3, 0, 1, 2, 4)
    arranged = arranged.reshape(n_ci, 2 * outer * rows * cols // 128, 128)
    parts = lax.all_to_all(arranged, CIRC, 0, 0, tiled=True)
    partial_value = parts.sum(axis=0).reshape(2, outer, rows, cols)
    arranged = partial_value.transpose(1, 0, 2, 3).reshape(outer, 2 * rows * cols // 128, 128)
    parts = lax.all_to_all(arranged, AXIAL[:-1], 0, 0, tiled=True)
    return parts.sum(axis=0).reshape(2, rows, cols)


def solution(mesh):
    sizes = [mesh.shape["axial"] // 16, 8, 2, mesh.shape["circ"] // 2, 2]
    fine = Mesh(mesh.devices.reshape(sizes), AXIAL + CIRC)
    in_specs = (
        P(AXIAL, CIRC, None, None),
        P(AXIAL, CIRC, None),
        P(AXIAL, CIRC, None, None),
        P(AXIAL, CIRC),
    )
    out_specs = P(None, AXIAL, CIRC)
    return jax.shard_map(body, mesh=fine, in_specs=in_specs, out_specs=out_specs, check_vma=False)
```

```python
import numpy as np
import ml_dtypes
import jax
import jax.numpy as jnp
from jax import lax
from jax.sharding import Mesh, PartitionSpec as P

ALONG = 16
AROUND = 8

axial_decay = 0.125
circ_decay = 0.16
wavenumber = 0.6

OFFSETS = ((0, 0), (0, 1), (1, -1), (1, 0), (1, 1))


def base_tiles():
    patch = np.arange(ALONG * AROUND)
    along_pos = (patch // AROUND).astype(np.float32)
    around_pos = (patch % AROUND).astype(np.float32)
    tiles = []
    for oa, oc in OFFSETS:
        gap_along = np.float32(oa * ALONG) + along_pos[None, :] - along_pos[:, None]
        gap_around = np.float32(oc * AROUND) + around_pos[None, :] - around_pos[:, None]
        envelope = np.exp(
            np.float32(-axial_decay) * np.abs(gap_along) - np.float32(circ_decay) * np.abs(gap_around)
        ).astype(np.float32)
        real_tile = envelope * np.cos(np.float32(wavenumber) * gap_along).astype(np.float32)
        imag_tile = -envelope * np.sin(np.float32(wavenumber) * gap_along).astype(np.float32)
        tiles.append(np.stack([real_tile, imag_tile]))
    return np.stack(tiles).astype(ml_dtypes.bfloat16)


AXIAL = ("y_hi", "z", "core")
CIRC = ("x", "y_lo")


def group_size(axes):
    return int(np.prod([lax.axis_size(a) for a in axes]))


def shifted(block, axes, moves):
    sizes = [group_size(a) for a in axes]
    total = int(np.prod(sizes))
    pairs = []
    for dst in range(total):
        coords = list(np.unravel_index(dst, sizes))
        ok = True
        for d, (move, cyclic) in enumerate(moves):
            c = coords[d] + move
            if cyclic:
                c %= sizes[d]
            elif not 0 <= c < sizes[d]:
                ok = False
            coords[d] = c
        if ok:
            src = int(np.ravel_multi_index(coords, sizes))
            pairs.append((src, dst))
    return lax.ppermute(block, sum(axes, ()), pairs)


def body(mode_shapes, amplitude, pair_list, pair_counts):
    along_blocks, around_blocks, patch_count, mode_count = mode_shapes.shape
    block_count = along_blocks * around_blocks
    weighted = (mode_shapes * amplitude[..., None]).astype(jnp.bfloat16)

    both = (AXIAL, CIRC)
    right = shifted(weighted[:, 0], (CIRC,), ((1, True),))
    left = shifted(weighted[1, 1], (CIRC,), ((-1, True),))
    ahead = shifted(weighted[0], (AXIAL,), ((1, False),))
    ahead_left = shifted(weighted[0, 1], both, ((1, False), (-1, True)))
    ahead_right = shifted(weighted[0, 0], both, ((1, False), (1, True)))

    def window(x, y):
        if x < 2 and 0 <= y < 2:
            return weighted[x, y]
        if x < 2 and y == 2:
            return right[x]
        if x == 1 and y == -1:
            return left
        if x == 2 and 0 <= y < 2:
            return ahead[y]
        if x == 2 and y == -1:
            return ahead_left
        return ahead_right

    columns = jnp.stack(
        [
            jnp.concatenate([window(i + oa, j + oc) for oa, oc in OFFSETS], axis=0)
            for i in range(along_blocks)
            for j in range(around_blocks)
        ]
    )

    listing = pair_list[0, 0]
    slot_total = listing.shape[1]
    slot = jnp.arange(slot_total, dtype=jnp.int32)
    valid = (slot < pair_counts[0, 0]).astype(jnp.float32)
    half = jnp.where((listing[1] == 0) & (listing[2] == 0), 0.5, 1.0).astype(jnp.float32)
    kind = listing[1] * 3 + listing[2]
    row_hot = (listing[0][None, :] == jnp.arange(block_count)[:, None]).astype(jnp.float32)
    kind_hot = (kind[None, :] == jnp.arange(len(OFFSETS))[:, None]).astype(jnp.float32)
    weight = jnp.einsum("rs,ks,s->rk", row_hot, kind_hot, valid * half)

    tiles = jnp.asarray(base_tiles())
    lhs = (tiles.astype(jnp.float32)[None] * weight[:, :, None, None, None]).astype(jnp.bfloat16)
    lhs = jnp.transpose(lhs, (0, 2, 3, 1, 4)).reshape(block_count, 2 * patch_count, -1)
    row_sums = lax.dot_general(
        lhs, columns, (((2,), (1,)), ((0,), (0,))), preferred_element_type=jnp.float32
    )
    rounded = row_sums.astype(jnp.bfloat16).reshape(block_count, 2, patch_count, mode_count)
    rounded = jnp.transpose(rounded, (1, 0, 2, 3)).reshape(2, block_count * patch_count, mode_count)
    local = weighted.reshape(block_count * patch_count, mode_count)
    first = jnp.stack([jnp.concatenate([local, rounded[q]], axis=0) for q in range(2)])
    second = jnp.stack(
        [jnp.concatenate([rounded[0], local], axis=0), jnp.concatenate([rounded[1], -local], axis=0)]
    )
    summand = lax.dot_general(
        first, second, (((1,), (1,)), ((0,), (0,))), preferred_element_type=jnp.float32
    )
    n_core = lax.axis_size("core")
    outer = group_size(AXIAL) // n_core
    n_ci = group_size(CIRC)
    cols = mode_count // n_ci
    rows = mode_count // (outer * n_core)
    split = summand.reshape(2, outer, n_core, rows, n_ci, cols).transpose(2, 4, 0, 1, 3, 5)
    split = split.reshape(n_core, n_ci, 2 * outer * rows * cols // 128, 128)
    mine = lax.axis_index("core")
    keep = lax.dynamic_index_in_dim(split, mine, axis=0, keepdims=False)
    send = lax.dynamic_index_in_dim(split, n_core - 1 - mine, axis=0, keepdims=False)
    pairs = [(k, n_core - 1 - k) for k in range(n_core)]
    arranged = keep + lax.ppermute(send, "core", pairs)
    parts = lax.all_to_all(arranged, CIRC, 0, 0, tiled=True)
    partial_value = parts.sum(axis=0).reshape(2, outer, rows, cols)
    arranged = partial_value.transpose(1, 0, 2, 3).reshape(outer, 2 * rows * cols // 128, 128)
    parts = lax.all_to_all(arranged, AXIAL[:-1], 0, 0, tiled=True)
    return parts.sum(axis=0).reshape(2, rows, cols)


def solution(mesh):
    sizes = [mesh.shape["axial"] // 16, 8, 2, mesh.shape["circ"] // 2, 2]
    fine = Mesh(mesh.devices.reshape(sizes), AXIAL + CIRC)
    in_specs = (
        P(AXIAL, CIRC, None, None),
        P(AXIAL, CIRC, None),
        P(AXIAL, CIRC, None, None),
        P(AXIAL, CIRC),
    )
    out_specs = P(None, AXIAL, CIRC)
    return jax.shard_map(body, mesh=fine, in_specs=in_specs, out_specs=out_specs, check_vma=False)
```

```python
import numpy as np
import ml_dtypes
import jax
import jax.numpy as jnp
from jax import lax
from jax.sharding import PartitionSpec as P

ALONG = 16
AROUND = 8

axial_decay = 0.125
circ_decay = 0.16
wavenumber = 0.6

OFFSETS = ((0, 0), (0, 1), (1, -1), (1, 0), (1, 1))


def base_tiles():
    patch = np.arange(ALONG * AROUND)
    along_pos = (patch // AROUND).astype(np.float32)
    around_pos = (patch % AROUND).astype(np.float32)
    tiles = []
    for oa, oc in OFFSETS:
        gap_along = np.float32(oa * ALONG) + along_pos[None, :] - along_pos[:, None]
        gap_around = np.float32(oc * AROUND) + around_pos[None, :] - around_pos[:, None]
        envelope = np.exp(
            np.float32(-axial_decay) * np.abs(gap_along) - np.float32(circ_decay) * np.abs(gap_around)
        ).astype(np.float32)
        real_tile = envelope * np.cos(np.float32(wavenumber) * gap_along).astype(np.float32)
        imag_tile = -envelope * np.sin(np.float32(wavenumber) * gap_along).astype(np.float32)
        tiles.append(np.stack([real_tile, imag_tile]))
    return np.stack(tiles).astype(ml_dtypes.bfloat16)


def shifted(block, axes, moves):
    sizes = [lax.axis_size(a) for a in axes]
    total = int(np.prod(sizes))
    pairs = []
    for dst in range(total):
        coords = list(np.unravel_index(dst, sizes))
        ok = True
        for d, (move, cyclic) in enumerate(moves):
            c = coords[d] + move
            if cyclic:
                c %= sizes[d]
            elif not 0 <= c < sizes[d]:
                ok = False
            coords[d] = c
        if ok:
            src = int(np.ravel_multi_index(coords, sizes))
            pairs.append((src, dst))
    return lax.ppermute(block, axes if len(axes) > 1 else axes[0], pairs)


def body(mode_shapes, amplitude, pair_list, pair_counts):
    along_blocks, around_blocks, patch_count, mode_count = mode_shapes.shape
    block_count = along_blocks * around_blocks
    weighted = (mode_shapes * amplitude[..., None]).astype(jnp.bfloat16)

    both = ("axial", "circ")
    right = shifted(weighted[:, 0], ("circ",), ((1, True),))
    left = shifted(weighted[1, 1], ("circ",), ((-1, True),))
    ahead = shifted(weighted[0], ("axial",), ((1, False),))
    ahead_left = shifted(weighted[0, 1], both, ((1, False), (-1, True)))
    ahead_right = shifted(weighted[0, 0], both, ((1, False), (1, True)))

    def window(x, y):
        if x < 2 and 0 <= y < 2:
            return weighted[x, y]
        if x < 2 and y == 2:
            return right[x]
        if x == 1 and y == -1:
            return left
        if x == 2 and 0 <= y < 2:
            return ahead[y]
        if x == 2 and y == -1:
            return ahead_left
        return ahead_right

    columns = jnp.stack(
        [
            jnp.concatenate([window(i + oa, j + oc) for oa, oc in OFFSETS], axis=0)
            for i in range(along_blocks)
            for j in range(around_blocks)
        ]
    )

    listing = pair_list[0, 0]
    slot_total = listing.shape[1]
    slot = jnp.arange(slot_total, dtype=jnp.int32)
    valid = (slot < pair_counts[0, 0]).astype(jnp.float32)
    half = jnp.where((listing[1] == 0) & (listing[2] == 0), 0.5, 1.0).astype(jnp.float32)
    kind = listing[1] * 3 + listing[2]
    row_hot = (listing[0][None, :] == jnp.arange(block_count)[:, None]).astype(jnp.float32)
    kind_hot = (kind[None, :] == jnp.arange(len(OFFSETS))[:, None]).astype(jnp.float32)
    weight = jnp.einsum("rs,ks,s->rk", row_hot, kind_hot, valid * half)

    tiles = jnp.asarray(base_tiles())
    lhs = (tiles.astype(jnp.float32)[None] * weight[:, :, None, None, None]).astype(jnp.bfloat16)
    lhs = jnp.transpose(lhs, (0, 2, 3, 1, 4)).reshape(block_count, 2 * patch_count, -1)
    row_sums = lax.dot_general(
        lhs, columns, (((2,), (1,)), ((0,), (0,))), preferred_element_type=jnp.float32
    )
    rounded = row_sums.astype(jnp.bfloat16).reshape(block_count, 2, patch_count, mode_count)
    rounded = jnp.transpose(rounded, (1, 0, 2, 3)).reshape(2, block_count * patch_count, mode_count)
    local = weighted.reshape(block_count * patch_count, mode_count)
    shared = jnp.stack(
        [jnp.concatenate([local, rounded[0], local], axis=0), jnp.concatenate([local, rounded[1], -local], axis=0)]
    )
    span = 2 * block_count * patch_count
    first = shared[:, :span]
    second = shared[:, block_count * patch_count :]
    summand = lax.dot_general(
        first, second, (((1,), (1,)), ((0,), (0,))), preferred_element_type=jnp.float32
    )
    n_ax = lax.axis_size("axial")
    n_ci = lax.axis_size("circ")
    cols = mode_count // n_ci
    rows = mode_count // n_ax
    parts = lax.all_to_all(
        summand.reshape(2, mode_count, n_ci, cols), "circ", 2, 0, tiled=True
    )
    partial_value = parts.reshape(n_ci, 2, mode_count, cols).sum(axis=0)
    arranged = partial_value.reshape(2, n_ax, rows, cols).transpose(1, 0, 2, 3)
    arranged = arranged.reshape(n_ax, 2 * rows * cols // 128, 128)
    parts = lax.all_to_all(arranged, "axial", 0, 0, tiled=True)
    return parts.sum(axis=0).reshape(2, rows, cols)


def solution(mesh):
    in_specs = (
        P("axial", "circ", None, None),
        P("axial", "circ", None),
        P("axial", "circ", None, None),
        P("axial", "circ"),
    )
    out_specs = P(None, "axial", "circ")
    return jax.shard_map(body, mesh=mesh, in_specs=in_specs, out_specs=out_specs, check_vma=False)
```
